256 devices in a mesh: ka: 16 (over z, y_lo), band: 8 (over x, y_hi), ga: 2 (over core).
Axes of the slice: x: 4, y: 4 (y_hi: 2, y_lo: 2; y = y_hi * 2 + y_lo), z: 8, core: 2. Of those that a mesh axis runs over, the one named last changes fastest.
Arguments:
- pair_density: bfloat16 [8, 256, 8, 2048], P(None, ('ka', 'band')), may hold values from -4 to 4
- valence_energy: float32 [8, 8], replicated, may hold values from -6 to -1
- conduction_energy: float32 [8, 256], replicated, may hold values from 0.5 to 12
- star_map: int32 [64], replicated, may hold values from 0 to 7, as said below
- op_of_k: int32 [64], replicated, may hold values from 0 to 47
- perm_lists: int32 [48, 2048], replicated, may hold values from 0 to 2047, as said below
- cond_top: int32 [64], replicated, may hold values from 128 to 256
Outputs:
- chi: float32 [1, 2048, 2048], P(None, ('band', 'ga'), 'ka')
The draws below stay inside these ranges and needn't reach their ends.
Inputs may be any that keep to these rules, and one draw needn't show every extreme that they name: `star_map`: every irreducible point is named by at least one full-zone k-point. `perm_lists`: each row is a permutation of 0 .. 2047 that maps every aligned block of 128 slots onto itself.
All inputs are finite; a program needn't handle non-finite values.
Results may differ from the reference program's by a relative error of at most 0.0015.
Values may be sent and summed in bfloat16 or wider, within the bound.
No kernel may reach another device: no remote copies, remote signals or barrier semaphores. Data moves between devices by JAX's collectives and lax.ppermute only.
A program may use at most 128 MiB of HBM per device.

```python
import jax
import jax.numpy as jnp
from jax import lax

NV = 8
NC = 256
NG = 2048
GB = 128
KI = 8
KF = 64
NOPS = 48
NF = 1


def draw_star_map(key, part):
    first_key, second_key = jax.random.split(jax.random.fold_in(key, 17))
    extra = jax.random.randint(first_key, (KF - KI,), 0, KI)
    base = jnp.concatenate([jnp.arange(KI), extra]).astype(jnp.int32)
    return jax.random.permutation(second_key, base).astype(jnp.int32)


def draw_cond_top(key, part):
    first_key, second_key = jax.random.split(jax.random.fold_in(key, 29))
    values = jax.random.randint(first_key, (KF,), NC // 2, NC + 1).astype(jnp.int32)
    places = jax.random.permutation(second_key, KF)
    values = values.at[places[0]].set(NC)
    values = values.at[places[1]].set(NC // 2)
    return values.astype(jnp.int32)


def draw_perm_lists(key, part):
    blocks = NG // GB
    keys = jax.random.split(jax.random.fold_in(key, 41), NOPS * blocks)
    shuffled = jax.vmap(lambda item: jax.random.permutation(item, GB))(keys)
    shuffled = shuffled.reshape(NOPS, blocks, GB) + (jnp.arange(blocks) * GB)[None, :, None]
    return shuffled.reshape(NOPS, NG).astype(jnp.int32)


def with_ends(entries, key, smallest, largest):
    index_at = [jax.random.randint(jax.random.fold_in(key, axis), (), 0, length) for axis, length in enumerate(entries.shape)]
    main_axis = entries.shape.index(max(entries.shape))
    next_to = index_at[:main_axis] + [(index_at[main_axis] + 1) % entries.shape[main_axis]] + index_at[main_axis + 1:]
    return entries.at[tuple(index_at)].set(smallest).at[tuple(next_to)].set(largest)


def block_scale(own_key, shape, cuts, smallest, top_value):
    def one(dim, shards_of):
        draws = jax.random.uniform(jax.random.fold_in(jax.random.fold_in(own_key, 6), dim), (shards_of,), jnp.float32, smallest / len(cuts), top_value / len(cuts))
        return jnp.repeat(jnp.exp(draws), shape[dim] // shards_of).reshape((-1,) + (1,) * (len(shape) - dim - 1))

    level = one(*cuts[0])
    for cut in cuts[1:]:
        level = level * one(*cut)
    return level


def scatter_about(rng, extent, spread, reach, shards=(), dtype=jnp.bfloat16):
    array = spread * jax.random.normal(rng, extent, jnp.float32)
    if shards:
        array = array * block_scale(rng, extent, shards, -0.22, 0.18)
    return jnp.clip(array, -reach, reach).astype(dtype)


def setup_inputs(seed: int = 0) -> dict:
    seeds = jax.random.split(jax.random.key(seed), 8)
    pair_density = scatter_about(seeds[0], (KI, NC, NV, NG), 0.5, 4.0, ((1, 128),))
    valence_energy = jnp.clip(jax.random.uniform(seeds[1], (KI, NV), jnp.float32, -6.0, -1.0), -6.0, -1.0)
    conduction_energy = jnp.clip(jax.random.uniform(seeds[2], (KI, NC), jnp.float32, 0.5, 12.0), 0.5, 12.0)
    star_map = draw_star_map(jax.random.fold_in(seeds[7], 71), 0)
    op_of_k = with_ends(jax.random.randint(seeds[4], (KF,), 0, NOPS), jax.random.fold_in(seeds[4], 1), 0, NOPS - 1).astype(jnp.int32)
    perm_lists = draw_perm_lists(jax.random.fold_in(seeds[7], 71), 0)
    cond_top = draw_cond_top(jax.random.fold_in(seeds[7], 71), 0)
    return dict(pair_density=pair_density, valence_energy=valence_energy, conduction_energy=conduction_energy, star_map=star_map, op_of_k=op_of_k, perm_lists=perm_lists, cond_top=cond_top)


freq_step = 2.0


def reference(pair_density, valence_energy, conduction_energy, star_map, op_of_k, perm_lists, cond_top):
    omega = freq_step * jnp.arange(NF).astype(jnp.float32)
    omega_sq = (omega * omega)[:, None, None]
    band_ids = jnp.arange(NC).astype(jnp.int32)

    def accumulate(chi_sum, kpoint):
        source = star_map[kpoint]
        block = pair_density[source]
        rotated = jnp.take(block, perm_lists[op_of_k[kpoint]], axis=2)
        diff = valence_energy[source][None, :] - conduction_energy[source][:, None]
        mask = (band_ids < cond_top[kpoint]).astype(jnp.float32)[None, :, None]
        weight = (4.0 / KF) * diff[None] / (diff[None] * diff[None] + omega_sq) * mask
        product = weight[..., None] * rotated.astype(jnp.float32)[None]
        scaled_hi = product.astype(jnp.bfloat16)
        hi_back = lax.optimization_barrier(scaled_hi).astype(jnp.float32)
        scaled_lo = (product - hi_back).astype(jnp.bfloat16)
        flat = rotated.reshape(NC * NV, NG).astype(jnp.float32)
        flat_hi = scaled_hi.reshape(NF, NC * NV, NG).astype(jnp.float32)
        flat_lo = scaled_lo.reshape(NF, NC * NV, NG).astype(jnp.float32)
        term = jnp.einsum("rg,frh->fgh", flat, flat_hi, precision=lax.Precision.HIGHEST)
        term = term + jnp.einsum("rg,frh->fgh", flat, flat_lo, precision=lax.Precision.HIGHEST)
        return chi_sum + term, None

    start = jnp.zeros((NF, NG, NG), jnp.float32)
    chi, unused = lax.scan(accumulate, start, jnp.arange(KF).astype(jnp.int32))
    return chi
```

```python
import jax
import jax.numpy as jnp
from jax import lax
from jax.sharding import PartitionSpec as P

NG = 2048
GB = 128
KI = 8
KF = 64
NF = 1
NV = 8

BW = 512
NB = NG // BW
PAIR = ((0, 1), (2, 3), (0, 1), (0, 2), (0, 3), (1, 2), (1, 3), (2, 3))
LOCAL = (((0, 0), (1, 1)), ((0, 0), (1, 1))) + (((0, 1), (1, 0)),) * 6


freq_step = 2.0


def slab_perm(ka_count, band_count, ga_count):
    pieces = BW // GB
    pairs = []
    for i in range(ka_count):
        for j in range(band_count):
            for g in range(ga_count):
                row_block = PAIR[j][LOCAL[j][g][0]]
                col_block = PAIR[j][LOCAL[j][g][1]]
                r = row_block * pieces + i // pieces
                cs = col_block * pieces + i % pieces
                src = (i * band_count + j) * ga_count + g
                dst = (cs * band_count + r // ga_count) * ga_count + r % ga_count
                pairs.append((src, dst))
    return pairs


def on_device(
    pair_density, valence_energy, conduction_energy, star_map, op_of_k, perm_lists, cond_top
):
    ka_count = lax.axis_size("ka")
    band_count = lax.axis_size("band")
    ga_count = lax.axis_size("ga")
    assert (ka_count, band_count, ga_count) == (16, 8, 2)
    ka_index = lax.axis_index("ka")
    band_index = lax.axis_index("band")
    ga_index = lax.axis_index("ga")
    cond_piece = pair_density.shape[1]
    pair = jnp.asarray(PAIR, jnp.int32)
    local_tab = jnp.asarray(LOCAL, jnp.int32)

    blocked = pair_density.reshape(KI, cond_piece, NV, NB, BW)
    send = jnp.take(blocked, pair.reshape(-1), axis=3)
    send = send.reshape(KI, cond_piece, NV, band_count, 2, BW)
    send = jnp.moveaxis(send, 3, 0)
    recv = lax.all_to_all(send, "band", 0, 0, tiled=False)
    c_loc = band_count * cond_piece
    loc = jnp.moveaxis(recv, 0, 1).reshape(KI, c_loc, NV, 2, BW)

    picked = jnp.take(loc, star_map, axis=0)
    my_pair = pair[band_index]
    perm_blocks = perm_lists.reshape(perm_lists.shape[0], NB, BW)
    my_perm = jnp.take(jnp.take(perm_blocks, op_of_k, axis=0), my_pair, axis=1)
    subs = BW // GB
    local = my_perm.reshape(KF, 2 * subs, GB) - (
        my_pair.repeat(subs) * BW + (jnp.arange(2 * subs) % subs) * GB
    )[None, :, None]
    onehot = (local[..., None] == jnp.arange(GB)[None, None, None, :]).astype(jnp.bfloat16)
    shaped = picked.reshape(KF, c_loc * NV, 2 * subs, GB)
    rotated = jnp.einsum("krbi,kboi->krbo", shaped, onehot, preferred_element_type=jnp.float32)
    rotated = rotated.astype(jnp.bfloat16).reshape(KF, c_loc, NV, 2, BW)

    c_base = ka_index * c_loc
    cond_grp = lax.dynamic_slice_in_dim(conduction_energy, c_base, c_loc, axis=1)
    cond_local = jnp.take(cond_grp, star_map, axis=0)
    val_local = jnp.take(valence_energy, star_map, axis=0)
    band_global = c_base + jnp.arange(c_loc)
    mask = (band_global[None, :] < cond_top[:, None]).astype(jnp.float32)[None, :, :, None]
    omega = freq_step * jnp.arange(NF).astype(jnp.float32)
    omega_sq = (omega * omega)[:, None, None, None]
    diff = val_local[:, None, :] - cond_local[:, :, None]
    weight = 4.0 / KF * diff[None] / (diff[None] * diff[None] + omega_sq) * mask

    row_sel = local_tab[band_index, ga_index, 0]
    col_sel = local_tab[band_index, ga_index, 1]
    rot_row = lax.dynamic_index_in_dim(rotated, row_sel, axis=3, keepdims=False)
    rot_col = lax.dynamic_index_in_dim(rotated, col_sel, axis=3, keepdims=False)
    product = weight[..., None] * rot_col[None].astype(jnp.float32)
    scaled_hi = product.astype(jnp.bfloat16)
    hi_back = lax.optimization_barrier(scaled_hi).astype(jnp.float32)
    scaled_lo = (product - hi_back).astype(jnp.bfloat16)
    pair_rows = KF * c_loc * NV
    flat_scaled = jnp.stack(
        [scaled_hi.reshape(NF, pair_rows, BW), scaled_lo.reshape(NF, pair_rows, BW)]
    )
    partial_value = jnp.einsum(
        "rg,sfrh->fgh", rot_row.reshape(pair_rows, BW), flat_scaled,
        preferred_element_type=jnp.float32,
    )

    pieces = partial_value.reshape(NF, subs, GB, subs, GB).transpose(1, 3, 0, 2, 4)
    pieces = pieces.reshape(subs * subs, NF, GB, GB)
    got = lax.all_to_all(pieces, "ka", 0, 0, tiled=False)
    slab = got.sum(axis=0)
    return lax.ppermute(
        slab, ("ka", "band", "ga"), slab_perm(ka_count, band_count, ga_count)
    )


def solution(mesh):
    return jax.shard_map(
        on_device,
        mesh=mesh,
        in_specs=(P(None, ("ka", "band"), None, None), P(), P(), P(), P(), P(), P()),
        out_specs=P(None, ("band", "ga"), "ka"),
        check_vma=False,
    )
```

```python
import jax
import jax.numpy as jnp
from jax import lax
from jax.experimental import pallas as pl
from jax.experimental.pallas import tpu as pltpu
from jax.sharding import PartitionSpec as P

NG = 2048
GB = 128
KI = 8
KF = 64
NF = 1
NV = 8

BW = 512
NB = NG // BW
PAIR = ((0, 1), (2, 3), (0, 1), (0, 2), (0, 3), (1, 2), (1, 3), (2, 3))
LOCAL = (((0, 0), (1, 1)), ((0, 0), (1, 1))) + (((0, 1), (1, 0)),) * 6
BLOCKS = tuple(
    tuple((PAIR[j][LOCAL[j][g][0]], PAIR[j][LOCAL[j][g][1]]) for g in range(2))
    for j in range(len(PAIR))
)
KB = 4


freq_step = 2.0


def chi_kernel(star_ref, loc_ref, perm_ref, w_ref, out_ref):
    step = pl.program_id(0)

    @pl.when(step == 0)
    def _():
        out_ref[...] = jnp.zeros_like(out_ref)

    lane = lax.broadcasted_iota(jnp.int32, (GB, GB), 1)
    nt = (((1,), (1,)), ((), ()))
    for t in range(KB):
        x = loc_ref[star_ref[step * KB + t]]
        slots = perm_ref[t]
        parts = []
        for q in range(2 * BW // GB):
            onehot = jnp.where(slots[:, q : q + 1] == lane, 1.0, 0.0).astype(jnp.bfloat16)
            parts.append(
                lax.dot_general(
                    onehot, x[:, q * GB : (q + 1) * GB], nt,
                    preferred_element_type=jnp.float32,
                )
            )
        rot_t = jnp.concatenate(parts, axis=0)
        row_t = rot_t[:BW].astype(jnp.bfloat16)
        col_t = rot_t[BW:]
        lhs = jnp.concatenate([row_t, row_t], axis=1)
        for f in range(NF):
            product = col_t * w_ref[t, f : f + 1, :]
            scaled_hi = product.astype(jnp.bfloat16)
            scaled_lo = (product - scaled_hi.astype(jnp.float32)).astype(jnp.bfloat16)
            rhs = jnp.concatenate([scaled_hi, scaled_lo], axis=1)
            out_ref[f] += lax.dot_general(lhs, rhs, nt, preferred_element_type=jnp.float32)


def chi_block(star_map, loc, perm_t, weight_t):
    rows = loc.shape[1]
    return pl.pallas_call(
        chi_kernel,
        out_shape=jax.ShapeDtypeStruct((NF, BW, BW), jnp.float32),
        grid_spec=pltpu.PrefetchScalarGridSpec(
            num_scalar_prefetch=1,
            grid=(KF // KB,),
            in_specs=[
                pl.BlockSpec((KI, rows, 2 * BW), lambda st, sm: (0, 0, 0)),
                pl.BlockSpec((KB, GB, 2 * BW // GB), lambda st, sm: (st, 0, 0)),
                pl.BlockSpec((KB, NF, rows), lambda st, sm: (st, 0, 0)),
            ],
            out_specs=pl.BlockSpec((NF, BW, BW), lambda st, sm: (0, 0, 0)),
        ),
        compiler_params=pltpu.CompilerParams(dimension_semantics=("arbitrary",)),
    )(star_map, loc, perm_t, weight_t)


def slab_perm(ka_count, band_count, ga_count):
    pieces = BW // GB
    pairs = []
    for i in range(ka_count):
        for j in range(band_count):
            for g in range(ga_count):
                row_block, col_block = BLOCKS[j][g]
                r = row_block * pieces + i // pieces
                cs = col_block * pieces + i % pieces
                src = (i * band_count + j) * ga_count + g
                dst = (cs * band_count + r // ga_count) * ga_count + r % ga_count
                pairs.append((src, dst))
    return pairs


def on_device(
    pair_density, valence_energy, conduction_energy, star_map, op_of_k, perm_lists, cond_top
):
    ka_count = lax.axis_size("ka")
    band_count = lax.axis_size("band")
    ga_count = lax.axis_size("ga")
    assert (ka_count, band_count, ga_count) == (16, 8, 2)
    ka_index = lax.axis_index("ka")
    band_index = lax.axis_index("band")
    ga_index = lax.axis_index("ga")
    cond_piece = pair_density.shape[1]
    blocks = jnp.asarray(BLOCKS, jnp.int32)

    blocked = pair_density.reshape(KI, cond_piece, NV, NB, BW)
    send = jnp.take(blocked, blocks[:, ga_index].reshape(-1), axis=3)
    send = send.reshape(KI, cond_piece, NV, band_count, 2, BW)
    send = jnp.moveaxis(send, 3, 0)
    recv = lax.all_to_all(send, "band", 0, 0, tiled=False)
    c_loc = band_count * cond_piece
    loc = jnp.moveaxis(recv, 0, 1).reshape(KI, c_loc * NV, 2 * BW)

    c_base = ka_index * c_loc
    cond_grp = lax.dynamic_slice_in_dim(conduction_energy, c_base, c_loc, axis=1)
    cond_local = jnp.take(cond_grp, star_map, axis=0)
    val_local = jnp.take(valence_energy, star_map, axis=0)
    band_global = c_base + jnp.arange(c_loc)
    mask = (band_global[None, :] < cond_top[:, None]).astype(jnp.float32)[None, :, :, None]
    omega = freq_step * jnp.arange(NF).astype(jnp.float32)
    omega_sq = (omega * omega)[:, None, None, None]
    diff = val_local[:, None, :] - cond_local[:, :, None]
    weight = 4.0 / KF * diff[None] / (diff[None] * diff[None] + omega_sq) * mask
    weight_t = jnp.transpose(weight.reshape(NF, KF, c_loc * NV), (1, 0, 2))

    my_blocks = blocks[band_index, ga_index]
    perm_blocks = perm_lists.reshape(perm_lists.shape[0], NB, BW)
    my_perm = jnp.take(jnp.take(perm_blocks, op_of_k, axis=0), my_blocks, axis=1)
    subs = BW // GB
    local = my_perm.reshape(KF, 2 * subs, GB) - (
        my_blocks.repeat(subs) * BW + (jnp.arange(2 * subs) % subs) * GB
    )[None, :, None]
    perm_t = jnp.transpose(local, (0, 2, 1))
    partial_value = chi_block(star_map, loc, perm_t, weight_t)

    pieces = partial_value.reshape(NF, subs, GB, subs, GB).transpose(1, 3, 0, 2, 4)
    pieces = pieces.reshape(subs * subs, NF, GB, GB)
    got = lax.all_to_all(pieces, "ka", 0, 0, tiled=False)
    slab = got.sum(axis=0)
    return lax.ppermute(
        slab, ("ka", "band", "ga"), slab_perm(ka_count, band_count, ga_count)
    )


def solution(mesh):
    return jax.shard_map(
        on_device,
        mesh=mesh,
        in_specs=(P(None, ("ka", "band"), None, None), P(), P(), P(), P(), P(), P()),
        out_specs=P(None, ("band", "ga"), "ka"),
        check_vma=False,
    )
```

```python
import jax
import jax.numpy as jnp
from jax import lax
from jax.experimental import pallas as pl
from jax.experimental.pallas import tpu as pltpu
from jax.sharding import PartitionSpec as P

NG = 2048
GB = 128
KI = 8
KF = 64
NF = 1
NV = 8

BW = 512
NB = NG // BW
PAIR = ((0, 1), (2, 3), (0, 1), (0, 2), (0, 3), (1, 2), (1, 3), (2, 3))
LOCAL = (((0, 0), (1, 1)), ((0, 0), (1, 1))) + (((0, 1), (1, 0)),) * 6
BLOCKS = tuple(
    tuple((PAIR[j][LOCAL[j][g][0]], PAIR[j][LOCAL[j][g][1]]) for g in range(2))
    for j in range(len(PAIR))
)
KB = 4


freq_step = 2.0


def chi_kernel(star_ref, loc_ref, perm_ref, perm_t_ref, w_ref, out_ref):
    step = pl.program_id(0)

    @pl.when(step == 0)
    def _():
        out_ref[...] = jnp.zeros_like(out_ref)

    lane = lax.broadcasted_iota(jnp.int32, (GB, GB), 1)
    sub = lax.broadcasted_iota(jnp.int32, (GB, GB), 0)
    nt = (((1,), (1,)), ((), ()))
    subs = BW // GB
    lhs_parts = []
    rhs_parts = [[] for _ in range(NF)]
    for t in range(KB):
        x = loc_ref[star_ref[step * KB + t]]
        slots_col = perm_t_ref[t]
        row_parts = []
        for q in range(subs):
            onehot = jnp.where(slots_col[:, q : q + 1] == lane, 1.0, 0.0).astype(jnp.bfloat16)
            row_parts.append(
                lax.dot_general(
                    onehot, x[:, q * GB : (q + 1) * GB], nt,
                    preferred_element_type=jnp.float32,
                )
            )
        row_t = jnp.concatenate(row_parts, axis=0).astype(jnp.bfloat16)
        slots_row = perm_ref[t]
        col_parts = []
        for q in range(subs, 2 * subs):
            onehot_t = jnp.where(slots_row[q : q + 1, :] == sub, 1.0, 0.0).astype(jnp.bfloat16)
            col_parts.append(
                jnp.dot(
                    x[:, q * GB : (q + 1) * GB], onehot_t,
                    preferred_element_type=jnp.float32,
                )
            )
        col = jnp.concatenate(col_parts, axis=1)
        lhs_parts += [row_t, row_t]
        for f in range(NF):
            product = col * w_ref[t][:, f : f + 1]
            scaled_hi = product.astype(jnp.bfloat16)
            scaled_lo = (product - scaled_hi.astype(jnp.float32)).astype(jnp.bfloat16)
            rhs_parts[f] += [scaled_hi, scaled_lo]
    lhs = jnp.concatenate(lhs_parts, axis=1)
    for f in range(NF):
        rhs = jnp.concatenate(rhs_parts[f], axis=0)
        out_ref[f] += jnp.dot(lhs, rhs, preferred_element_type=jnp.float32)


def chi_block(star_map, loc, perm, perm_t, weight_c):
    rows = loc.shape[1]
    return pl.pallas_call(
        chi_kernel,
        out_shape=jax.ShapeDtypeStruct((NF, BW, BW), jnp.float32),
        grid_spec=pltpu.PrefetchScalarGridSpec(
            num_scalar_prefetch=1,
            grid=(KF // KB,),
            in_specs=[
                pl.BlockSpec((KI, rows, 2 * BW), lambda st, sm: (0, 0, 0)),
                pl.BlockSpec((KB, 2 * BW // GB, GB), lambda st, sm: (st, 0, 0)),
                pl.BlockSpec((KB, GB, 2 * BW // GB), lambda st, sm: (st, 0, 0)),
                pl.BlockSpec((KB, rows, NF), lambda st, sm: (st, 0, 0)),
            ],
            out_specs=pl.BlockSpec((NF, BW, BW), lambda st, sm: (0, 0, 0)),
        ),
        compiler_params=pltpu.CompilerParams(dimension_semantics=("arbitrary",)),
    )(star_map, loc, perm, perm_t, weight_c)


def slab_perm(ka_count, band_count, ga_count):
    pieces = BW // GB
    pairs = []
    for i in range(ka_count):
        for j in range(band_count):
            for g in range(ga_count):
                row_block, col_block = BLOCKS[j][g]
                r = row_block * pieces + i // pieces
                cs = col_block * pieces + i % pieces
                src = (i * band_count + j) * ga_count + g
                dst = (cs * band_count + r // ga_count) * ga_count + r % ga_count
                pairs.append((src, dst))
    return pairs


def on_device(
    pair_density, valence_energy, conduction_energy, star_map, op_of_k, perm_lists, cond_top
):
    ka_count = lax.axis_size("ka")
    band_count = lax.axis_size("band")
    ga_count = lax.axis_size("ga")
    assert (ka_count, band_count, ga_count) == (16, 8, 2)
    ka_index = lax.axis_index("ka")
    band_index = lax.axis_index("band")
    ga_index = lax.axis_index("ga")
    cond_piece = pair_density.shape[1]
    blocks = jnp.asarray(BLOCKS, jnp.int32)

    blocked = pair_density.reshape(KI, cond_piece, NV, NB, BW)
    send = jnp.take(blocked, blocks[:, ga_index].reshape(-1), axis=3)
    send = send.reshape(KI, cond_piece, NV, band_count, 2, BW)
    send = jnp.moveaxis(send, 3, 0)
    recv = lax.all_to_all(send, "band", 0, 0, tiled=False)
    c_loc = band_count * cond_piece
    loc = jnp.moveaxis(recv, 0, 1).reshape(KI, c_loc * NV, 2 * BW)

    c_base = ka_index * c_loc
    cond_grp = lax.dynamic_slice_in_dim(conduction_energy, c_base, c_loc, axis=1)
    cond_local = jnp.take(cond_grp, star_map, axis=0)
    val_local = jnp.take(valence_energy, star_map, axis=0)
    band_global = c_base + jnp.arange(c_loc)
    mask = (band_global[None, :] < cond_top[:, None]).astype(jnp.float32)[None, :, :, None]
    omega = freq_step * jnp.arange(NF).astype(jnp.float32)
    omega_sq = (omega * omega)[:, None, None, None]
    diff = val_local[:, None, :] - cond_local[:, :, None]
    weight = 4.0 / KF * diff[None] / (diff[None] * diff[None] + omega_sq) * mask
    weight_c = jnp.transpose(weight.reshape(NF, KF, c_loc * NV), (1, 2, 0))

    my_blocks = blocks[band_index, ga_index]
    perm_blocks = perm_lists.reshape(perm_lists.shape[0], NB, BW)
    my_perm = jnp.take(jnp.take(perm_blocks, op_of_k, axis=0), my_blocks, axis=1)
    subs = BW // GB
    local = my_perm.reshape(KF, 2 * subs, GB) - (
        my_blocks.repeat(subs) * BW + (jnp.arange(2 * subs) % subs) * GB
    )[None, :, None]
    perm_t = jnp.transpose(local, (0, 2, 1))
    partial_value = chi_block(star_map, loc, local, perm_t, weight_c)

    pieces = partial_value.reshape(NF, subs, GB, subs, GB).transpose(1, 3, 0, 2, 4)
    pieces = pieces.reshape(subs * subs, NF, GB, GB)
    got = lax.all_to_all(pieces, "ka", 0, 0, tiled=False)
    slab = got.sum(axis=0)
    return lax.ppermute(
        slab, ("ka", "band", "ga"), slab_perm(ka_count, band_count, ga_count)
    )


def solution(mesh):
    return jax.shard_map(
        on_device,
        mesh=mesh,
        in_specs=(P(None, ("ka", "band"), None, None), P(), P(), P(), P(), P(), P()),
        out_specs=P(None, ("band", "ga"), "ka"),
        check_vma=False,
    )
```

```python
import functools

import jax
import jax.numpy as jnp
from jax import lax
from jax.experimental import pallas as pl
from jax.experimental.pallas import tpu as pltpu
from jax.sharding import PartitionSpec as P

NG = 2048
GB = 128
KI = 8
KF = 64
NF = 1
NV = 8

BW = 512
NB = NG // BW
PAIR = ((0, 1), (2, 3), (0, 1), (0, 2), (0, 3), (1, 2), (1, 3), (2, 3))
LOCAL = (((0, 0), (1, 1)), ((0, 0), (1, 1))) + (((0, 1), (1, 0)),) * 6
BLOCKS = tuple(
    tuple((PAIR[j][LOCAL[j][g][0]], PAIR[j][LOCAL[j][g][1]]) for g in range(2))
    for j in range(len(PAIR))
)
KB = 4


freq_step = 2.0


def chi_kernel(half, star_ref, loc_ref, perm_ref, perm_t_ref, w_ref, out_ref):
    step = pl.program_id(0)
    rows_half = GB // 2

    @pl.when(step == 0)
    def _():
        out_ref[...] = jnp.zeros_like(out_ref)

    lane = lax.broadcasted_iota(jnp.int32, (rows_half, GB), 1)
    sub = lax.broadcasted_iota(jnp.int32, (GB, GB), 0)
    nt = (((1,), (1,)), ((), ()))
    subs = BW // GB
    lhs_parts = []
    rhs_parts = [[] for _ in range(NF)]
    for t in range(KB):
        x = loc_ref[star_ref[step * KB + t]]
        slots_col = perm_t_ref[t, half * rows_half : (half + 1) * rows_half, :]
        row_parts = []
        for q in range(subs):
            onehot = jnp.where(slots_col[:, q : q + 1] == lane, 1.0, 0.0).astype(jnp.bfloat16)
            row_parts.append(
                lax.dot_general(
                    onehot, x[:, q * GB : (q + 1) * GB], nt,
                    preferred_element_type=jnp.float32,
                )
            )
        row_t = jnp.concatenate(row_parts, axis=0).astype(jnp.bfloat16)
        slots_row = perm_ref[t]
        col_parts = []
        for q in range(subs, 2 * subs):
            onehot_t = jnp.where(slots_row[q : q + 1, :] == sub, 1.0, 0.0).astype(jnp.bfloat16)
            col_parts.append(
                jnp.dot(
                    x[:, q * GB : (q + 1) * GB], onehot_t,
                    preferred_element_type=jnp.float32,
                )
            )
        col = jnp.concatenate(col_parts, axis=1)
        lhs_parts += [row_t, row_t]
        for f in range(NF):
            product = col * w_ref[t][:, f : f + 1]
            scaled_hi = product.astype(jnp.bfloat16)
            scaled_lo = (product - scaled_hi.astype(jnp.float32)).astype(jnp.bfloat16)
            rhs_parts[f] += [scaled_hi, scaled_lo]
    lhs = jnp.concatenate(lhs_parts, axis=1)
    for f in range(NF):
        rhs = jnp.concatenate(rhs_parts[f], axis=0)
        out_ref[f] += jnp.dot(lhs, rhs, preferred_element_type=jnp.float32)


def chi_block(half, star_map, loc, perm, perm_t, weight_c):
    rows = loc.shape[1]
    return pl.pallas_call(
        functools.partial(chi_kernel, half),
        out_shape=jax.ShapeDtypeStruct((NF, BW // 2, BW), jnp.float32),
        grid_spec=pltpu.PrefetchScalarGridSpec(
            num_scalar_prefetch=1,
            grid=(KF // KB,),
            in_specs=[
                pl.BlockSpec((KI, rows, 2 * BW), lambda st, sm: (0, 0, 0)),
                pl.BlockSpec((KB, 2 * BW // GB, GB), lambda st, sm: (st, 0, 0)),
                pl.BlockSpec((KB, GB, 2 * BW // GB), lambda st, sm: (st, 0, 0)),
                pl.BlockSpec((KB, rows, NF), lambda st, sm: (st, 0, 0)),
            ],
            out_specs=pl.BlockSpec((NF, BW // 2, BW), lambda st, sm: (0, 0, 0)),
        ),
        compiler_params=pltpu.CompilerParams(dimension_semantics=("arbitrary",)),
    )(star_map, loc, perm, perm_t, weight_c)


def slab_perm(ka_count, band_count, ga_count):
    pieces = BW // GB
    pairs = []
    for i in range(ka_count):
        for j in range(band_count):
            for g in range(ga_count):
                row_block, col_block = BLOCKS[j][g]
                r = row_block * pieces + i // pieces
                cs = col_block * pieces + i % pieces
                src = (i * band_count + j) * ga_count + g
                dst = (cs * band_count + r // ga_count) * ga_count + r % ga_count
                pairs.append((src, dst))
    return pairs


def on_device(
    pair_density, valence_energy, conduction_energy, star_map, op_of_k, perm_lists, cond_top
):
    ka_count = lax.axis_size("ka")
    band_count = lax.axis_size("band")
    ga_count = lax.axis_size("ga")
    assert (ka_count, band_count, ga_count) == (16, 8, 2)
    ka_index = lax.axis_index("ka")
    band_index = lax.axis_index("band")
    ga_index = lax.axis_index("ga")
    cond_piece = pair_density.shape[1]
    blocks = jnp.asarray(BLOCKS, jnp.int32)

    blocked = pair_density.reshape(KI, cond_piece, NV, NB, BW)
    send = jnp.take(blocked, blocks[:, ga_index].reshape(-1), axis=3)
    send = send.reshape(KI, cond_piece, NV, band_count, 2, BW)
    send = jnp.moveaxis(send, 3, 0)
    recv = lax.all_to_all(send, "band", 0, 0, tiled=False)
    c_loc = band_count * cond_piece
    loc = jnp.moveaxis(recv, 0, 1).reshape(KI, c_loc * NV, 2 * BW)

    c_base = ka_index * c_loc
    cond_grp = lax.dynamic_slice_in_dim(conduction_energy, c_base, c_loc, axis=1)
    cond_local = jnp.take(cond_grp, star_map, axis=0)
    val_local = jnp.take(valence_energy, star_map, axis=0)
    band_global = c_base + jnp.arange(c_loc)
    mask = (band_global[None, :] < cond_top[:, None]).astype(jnp.float32)[None, :, :, None]
    omega = freq_step * jnp.arange(NF).astype(jnp.float32)
    omega_sq = (omega * omega)[:, None, None, None]
    diff = val_local[:, None, :] - cond_local[:, :, None]
    weight = 4.0 / KF * diff[None] / (diff[None] * diff[None] + omega_sq) * mask
    weight_c = jnp.transpose(weight.reshape(NF, KF, c_loc * NV), (1, 2, 0))

    my_blocks = blocks[band_index, ga_index]
    perm_blocks = perm_lists.reshape(perm_lists.shape[0], NB, BW)
    my_perm = jnp.take(jnp.take(perm_blocks, op_of_k, axis=0), my_blocks, axis=1)
    subs = BW // GB
    local = my_perm.reshape(KF, 2 * subs, GB) - (
        my_blocks.repeat(subs) * BW + (jnp.arange(2 * subs) % subs) * GB
    )[None, :, None]
    perm_t = jnp.transpose(local, (0, 2, 1))
    halves = []
    for half in range(2):
        part = chi_block(half, star_map, loc, local, perm_t, weight_c)
        pieces = part.reshape(NF, subs, GB // 2, subs, GB).transpose(1, 3, 0, 2, 4)
        pieces = pieces.reshape(subs * subs, NF, GB // 2, GB)
        got = lax.all_to_all(pieces, "ka", 0, 0, tiled=False)
        halves.append(got.sum(axis=0))
    slab = jnp.concatenate(halves, axis=1)
    return lax.ppermute(
        slab, ("ka", "band", "ga"), slab_perm(ka_count, band_count, ga_count)
    )


def solution(mesh):
    return jax.shard_map(
        on_device,
        mesh=mesh,
        in_specs=(P(None, ("ka", "band"), None, None), P(), P(), P(), P(), P(), P()),
        out_specs=P(None, ("band", "ga"), "ka"),
        check_vma=False,
    )
```

```python
import jax
import jax.numpy as jnp
from jax import lax
from jax.experimental import pallas as pl
from jax.experimental.pallas import tpu as pltpu
from jax.sharding import PartitionSpec as P

NG = 2048
GB = 128
KI = 8
KF = 64
NF = 1
NV = 8

BW = 512
NB = NG // BW
PAIR = ((0, 1), (2, 3), (0, 1), (0, 2), (0, 3), (1, 2), (1, 3), (2, 3))
LOCAL = (((0, 0), (1, 1)), ((0, 0), (1, 1))) + (((0, 1), (1, 0)),) * 6
BLOCKS = tuple(
    tuple((PAIR[j][LOCAL[j][g][0]], PAIR[j][LOCAL[j][g][1]]) for g in range(2))
    for j in range(len(PAIR))
)
KB = 4


freq_step = 2.0


def chi_kernel(star_ref, loc_ref, onehot_ref, w_ref, out_ref):
    step = pl.program_id(0)

    @pl.when(step == 0)
    def _():
        out_ref[...] = jnp.zeros_like(out_ref)

    nt = (((1,), (1,)), ((), ()))
    subs = BW // GB
    lhs_parts = []
    rhs_parts = [[] for _ in range(NF)]
    for t in range(KB):
        x = loc_ref[star_ref[step * KB + t]]
        row_parts = []
        for q in range(subs):
            row_parts.append(
                lax.dot_general(
                    onehot_ref[t, q], x[:, q * GB : (q + 1) * GB], nt,
                    preferred_element_type=jnp.float32,
                )
            )
        row_t = jnp.concatenate(row_parts, axis=0).astype(jnp.bfloat16)
        col_parts = []
        for q in range(subs, 2 * subs):
            col_parts.append(
                jnp.dot(
                    x[:, q * GB : (q + 1) * GB], onehot_ref[t, q],
                    preferred_element_type=jnp.float32,
                )
            )
        col = jnp.concatenate(col_parts, axis=1)
        lhs_parts += [row_t, row_t]
        for f in range(NF):
            product = col * w_ref[t][:, f : f + 1]
            scaled_hi = product.astype(jnp.bfloat16)
            scaled_lo = (product - scaled_hi.astype(jnp.float32)).astype(jnp.bfloat16)
            rhs_parts[f] += [scaled_hi, scaled_lo]
    lhs = jnp.concatenate(lhs_parts, axis=1)
    for f in range(NF):
        rhs = jnp.concatenate(rhs_parts[f], axis=0)
        out_ref[f] += jnp.dot(lhs, rhs, preferred_element_type=jnp.float32)


def chi_block(star_map, loc, onehot, weight_c):
    rows = loc.shape[1]
    return pl.pallas_call(
        chi_kernel,
        out_shape=jax.ShapeDtypeStruct((NF, BW, BW), jnp.float32),
        grid_spec=pltpu.PrefetchScalarGridSpec(
            num_scalar_prefetch=1,
            grid=(KF // KB,),
            in_specs=[
                pl.BlockSpec((KI, rows, 2 * BW), lambda st, sm: (0, 0, 0)),
                pl.BlockSpec((KB, 2 * BW // GB, GB, GB), lambda st, sm: (st, 0, 0, 0)),
                pl.BlockSpec((KB, rows, NF), lambda st, sm: (st, 0, 0)),
            ],
            out_specs=pl.BlockSpec((NF, BW, BW), lambda st, sm: (0, 0, 0)),
        ),
        compiler_params=pltpu.CompilerParams(dimension_semantics=("arbitrary",)),
    )(star_map, loc, onehot, weight_c)


def slab_perm(ka_count, band_count, ga_count):
    pieces = BW // GB
    pairs = []
    for i in range(ka_count):
        for j in range(band_count):
            for g in range(ga_count):
                row_block, col_block = BLOCKS[j][g]
                r = row_block * pieces + i // pieces
                cs = col_block * pieces + i % pieces
                src = (i * band_count + j) * ga_count + g
                dst = (cs * band_count + r // ga_count) * ga_count + r % ga_count
                pairs.append((src, dst))
    return pairs


def on_device(
    pair_density, valence_energy, conduction_energy, star_map, op_of_k, perm_lists, cond_top
):
    ka_count = lax.axis_size("ka")
    band_count = lax.axis_size("band")
    ga_count = lax.axis_size("ga")
    assert (ka_count, band_count, ga_count) == (16, 8, 2)
    ka_index = lax.axis_index("ka")
    band_index = lax.axis_index("band")
    ga_index = lax.axis_index("ga")
    cond_piece = pair_density.shape[1]
    blocks = jnp.asarray(BLOCKS, jnp.int32)

    blocked = pair_density.reshape(KI, cond_piece, NV, NB, BW)
    send = jnp.take(blocked, blocks[:, ga_index].reshape(-1), axis=3)
    send = send.reshape(KI, cond_piece, NV, band_count, 2, BW)
    send = jnp.moveaxis(send, 3, 0)
    recv = lax.all_to_all(send, "band", 0, 0, tiled=False)
    c_loc = band_count * cond_piece
    loc = jnp.moveaxis(recv, 0, 1).reshape(KI, c_loc * NV, 2 * BW)

    c_base = ka_index * c_loc
    cond_grp = lax.dynamic_slice_in_dim(conduction_energy, c_base, c_loc, axis=1)
    cond_local = jnp.take(cond_grp, star_map, axis=0)
    val_local = jnp.take(valence_energy, star_map, axis=0)
    band_global = c_base + jnp.arange(c_loc)
    mask = (band_global[None, :] < cond_top[:, None]).astype(jnp.float32)[None, :, :, None]
    omega = freq_step * jnp.arange(NF).astype(jnp.float32)
    omega_sq = (omega * omega)[:, None, None, None]
    diff = val_local[:, None, :] - cond_local[:, :, None]
    weight = 4.0 / KF * diff[None] / (diff[None] * diff[None] + omega_sq) * mask
    weight_c = jnp.transpose(weight.reshape(NF, KF, c_loc * NV), (1, 2, 0))

    my_blocks = blocks[band_index, ga_index]
    perm_blocks = perm_lists.reshape(perm_lists.shape[0], NB, BW)
    my_perm = jnp.take(jnp.take(perm_blocks, op_of_k, axis=0), my_blocks, axis=1)
    subs = BW // GB
    local = my_perm.reshape(KF, 2 * subs, GB) - (
        my_blocks.repeat(subs) * BW + (jnp.arange(2 * subs) % subs) * GB
    )[None, :, None]
    slot = jnp.arange(GB)
    row_side = local[:, :subs, :, None] == slot[None, None, None, :]
    col_side = local[:, subs:, None, :] == slot[None, None, :, None]
    onehot = jnp.concatenate([row_side, col_side], axis=1).astype(jnp.bfloat16)
    partial_value = chi_block(star_map, loc, onehot, weight_c)

    pieces = partial_value.reshape(NF, subs, GB, subs, GB).transpose(1, 3, 0, 2, 4)
    pieces = pieces.reshape(subs * subs, NF, GB, GB)
    got = lax.all_to_all(pieces, "ka", 0, 0, tiled=False)
    slab = got.sum(axis=0)
    return lax.ppermute(
        slab, ("ka", "band", "ga"), slab_perm(ka_count, band_count, ga_count)
    )


def solution(mesh):
    return jax.shard_map(
        on_device,
        mesh=mesh,
        in_specs=(P(None, ("ka", "band"), None, None), P(), P(), P(), P(), P(), P()),
        out_specs=P(None, ("band", "ga"), "ka"),
        check_vma=False,
    )
```

```python
import jax
import jax.numpy as jnp
from jax import lax
from jax.experimental import pallas as pl
from jax.experimental.pallas import tpu as pltpu
from jax.sharding import PartitionSpec as P


NG = 2048
GB = 128
KI = 8
KF = 64
NF = 1
NV = 8

BW = 512
NB = NG // BW
PAIR = ((0, 1), (2, 3), (0, 1), (0, 2), (0, 3), (1, 2), (1, 3), (2, 3))
LOCAL = (((0, 0), (1, 1)), ((0, 0), (1, 1))) + (((0, 1), (1, 0)),) * 6
BLOCKS = tuple(
    tuple((PAIR[j][LOCAL[j][g][0]], PAIR[j][LOCAL[j][g][1]]) for g in range(2))
    for j in range(len(PAIR))
)
KB = 8


freq_step = 2.0


def chi_kernel(star_ref, loc_ref, onehot_ref, w_ref, *refs):
    step = pl.program_id(0)
    out_ref = refs[-1]

    @pl.when(step == 0)
    def _():
        if len(refs) == 2:
            out_ref[...] = refs[0][...]
        else:
            out_ref[...] = jnp.zeros_like(out_ref)

    nt = (((1,), (1,)), ((), ()))
    subs = BW // GB
    lhs_parts = []
    rhs_parts = [[] for _ in range(NF)]
    for t in range(KB):
        x = loc_ref[star_ref[step * KB + t]]
        row_parts = []
        for q in range(subs):
            row_parts.append(
                lax.dot_general(
                    onehot_ref[t, q], x[:, q * GB : (q + 1) * GB], nt,
                    preferred_element_type=jnp.float32,
                )
            )
        row_t = jnp.concatenate(row_parts, axis=0).astype(jnp.bfloat16)
        col_parts = []
        for q in range(subs, 2 * subs):
            col_parts.append(
                jnp.dot(
                    x[:, q * GB : (q + 1) * GB], onehot_ref[t, q],
                    preferred_element_type=jnp.float32,
                )
            )
        col = jnp.concatenate(col_parts, axis=1)
        lhs_parts += [row_t, row_t]
        for f in range(NF):
            product = col * w_ref[t][:, f : f + 1]
            scaled_hi = product.astype(jnp.bfloat16)
            scaled_lo = (product - scaled_hi.astype(jnp.float32)).astype(jnp.bfloat16)
            rhs_parts[f] += [scaled_hi, scaled_lo]
    lhs = jnp.concatenate(lhs_parts, axis=1)
    for f in range(NF):
        rhs = jnp.concatenate(rhs_parts[f], axis=0)
        out_ref[f] += jnp.dot(lhs, rhs, preferred_element_type=jnp.float32)


def chi_block(star_map, loc, onehot, weight_c, start=None):
    rows = loc.shape[1]
    extra = [] if start is None else [start]
    extra_specs = [pl.BlockSpec((NF, BW, BW), lambda st, sm: (0, 0, 0))] * len(extra)
    return pl.pallas_call(
        chi_kernel,
        out_shape=jax.ShapeDtypeStruct((NF, BW, BW), jnp.float32),
        grid_spec=pltpu.PrefetchScalarGridSpec(
            num_scalar_prefetch=1,
            grid=(KF // KB,),
            in_specs=[
                pl.BlockSpec((KI, rows, 2 * BW), lambda st, sm: (0, 0, 0)),
                pl.BlockSpec((KB, 2 * BW // GB, GB, GB), lambda st, sm: (st, 0, 0, 0)),
                pl.BlockSpec((KB, rows, NF), lambda st, sm: (st, 0, 0)),
            ]
            + extra_specs,
            out_specs=pl.BlockSpec((NF, BW, BW), lambda st, sm: (0, 0, 0)),
        ),
        compiler_params=pltpu.CompilerParams(dimension_semantics=("arbitrary",)),
    )(star_map, loc, onehot, weight_c, *extra)


def slab_perm(ka_count, band_count, ga_count):
    pieces = BW // GB
    pairs = []
    for i in range(ka_count):
        for j in range(band_count):
            for g in range(ga_count):
                row_block, col_block = BLOCKS[j][g]
                r = row_block * pieces + i // pieces
                cs = col_block * pieces + i % pieces
                src = (i * band_count + j) * ga_count + g
                dst = (cs * band_count + r // ga_count) * ga_count + r % ga_count
                pairs.append((src, dst))
    return pairs


def on_device(
    pair_density, valence_energy, conduction_energy, star_map, op_of_k, perm_lists, cond_top
):
    ka_count = lax.axis_size("ka")
    band_count = lax.axis_size("band")
    ga_count = lax.axis_size("ga")
    assert (ka_count, band_count, ga_count) == (16, 8, 2)
    ka_index = lax.axis_index("ka")
    band_index = lax.axis_index("band")
    ga_index = lax.axis_index("ga")
    cond_piece = pair_density.shape[1]
    blocks = jnp.asarray(BLOCKS, jnp.int32)

    blocked = pair_density.reshape(KI, cond_piece, NV, NB, BW)
    send = jnp.take(blocked, blocks[:, ga_index].reshape(-1), axis=3)
    send = send.reshape(KI, cond_piece, NV, band_count, 2, BW)
    send = jnp.moveaxis(send, 3, 0)
    c_loc = band_count * cond_piece
    v_half = NV // 2
    locs = []
    for h in range(2):
        recv = lax.all_to_all(
            send[:, :, :, h * v_half : (h + 1) * v_half], "band", 0, 0, tiled=False
        )
        locs.append(jnp.moveaxis(recv, 0, 1).reshape(KI, c_loc * v_half, 2 * BW))

    c_base = ka_index * c_loc
    cond_grp = lax.dynamic_slice_in_dim(conduction_energy, c_base, c_loc, axis=1)
    cond_local = jnp.take(cond_grp, star_map, axis=0)
    val_local = jnp.take(valence_energy, star_map, axis=0)
    band_global = c_base + jnp.arange(c_loc)
    mask = (band_global[None, :] < cond_top[:, None]).astype(jnp.float32)[None, :, :, None]
    omega = freq_step * jnp.arange(NF).astype(jnp.float32)
    omega_sq = (omega * omega)[:, None, None, None]
    diff = val_local[:, None, :] - cond_local[:, :, None]
    weight = 4.0 / KF * diff[None] / (diff[None] * diff[None] + omega_sq) * mask
    weight_c = jnp.transpose(weight, (1, 2, 3, 0))

    my_blocks = blocks[band_index, ga_index]
    perm_blocks = perm_lists.reshape(perm_lists.shape[0], NB, BW)
    my_perm = jnp.take(jnp.take(perm_blocks, op_of_k, axis=0), my_blocks, axis=1)
    subs = BW // GB
    local = my_perm.reshape(KF, 2 * subs, GB) - (
        my_blocks.repeat(subs) * BW + (jnp.arange(2 * subs) % subs) * GB
    )[None, :, None]
    slot = jnp.arange(GB)
    row_side = local[:, :subs, :, None] == slot[None, None, None, :]
    col_side = local[:, subs:, None, :] == slot[None, None, :, None]
    onehot = jnp.concatenate([row_side, col_side], axis=1).astype(jnp.bfloat16)
    partial_value = None
    for h in range(2):
        weight_h = weight_c[:, :, h * v_half : (h + 1) * v_half].reshape(KF, c_loc * v_half, NF)
        partial_value = chi_block(star_map, locs[h], onehot, weight_h, partial_value)

    pieces = partial_value.reshape(NF, subs, GB, subs, GB).transpose(1, 3, 0, 2, 4)
    pieces = pieces.reshape(subs * subs, NF, GB, GB)
    got = lax.all_to_all(pieces, "ka", 0, 0, tiled=False)
    slab = got.sum(axis=0)
    return lax.ppermute(
        slab, ("ka", "band", "ga"), slab_perm(ka_count, band_count, ga_count)
    )


def solution(mesh):
    return jax.shard_map(
        on_device,
        mesh=mesh,
        in_specs=(P(None, ("ka", "band"), None, None), P(), P(), P(), P(), P(), P()),
        out_specs=P(None, ("band", "ga"), "ka"),
        check_vma=False,
    )
```

```python
import jax
import jax.numpy as jnp
from jax import lax
from jax.experimental import pallas as pl
from jax.experimental.pallas import tpu as pltpu
from jax.sharding import PartitionSpec as P

NG = 2048
GB = 128
KI = 8
KF = 64
NF = 1
NV = 8

BW = 512
NB = NG // BW
PAIR = ((0, 1), (2, 3), (0, 1), (0, 2), (0, 3), (1, 2), (1, 3), (2, 3))
LOCAL = (((0, 0), (1, 1)), ((0, 0), (1, 1))) + (((0, 1), (1, 0)),) * 6
BLOCKS = tuple(
    tuple((PAIR[j][LOCAL[j][g][0]], PAIR[j][LOCAL[j][g][1]]) for g in range(2))
    for j in range(len(PAIR))
)
KB = 8


freq_step = 2.0


def chi_kernel(star_ref, loc_ref, onehot_ref, w_ref, out_ref, acc_ref):
    step = pl.program_id(0)

    @pl.when(step == 0)
    def _():
        acc_ref[...] = jnp.zeros_like(acc_ref)

    nt = (((1,), (1,)), ((), ()))
    subs = BW // GB
    lhs_parts = []
    rhs_parts = [[] for _ in range(NF)]
    for t in range(KB):
        x = loc_ref[:, star_ref[step * KB + t]]
        x = x.reshape(x.shape[0] * x.shape[1], x.shape[2])
        row_parts = []
        for q in range(subs):
            row_parts.append(
                lax.dot_general(
                    onehot_ref[t, q], x[:, q * GB : (q + 1) * GB], nt,
                    preferred_element_type=jnp.float32,
                )
            )
        row_t = jnp.concatenate(row_parts, axis=0).astype(jnp.bfloat16)
        col_parts = []
        for q in range(subs, 2 * subs):
            col_parts.append(
                jnp.dot(
                    x[:, q * GB : (q + 1) * GB], onehot_ref[t, q],
                    preferred_element_type=jnp.float32,
                )
            )
        col = jnp.concatenate(col_parts, axis=1)
        lhs_parts += [row_t, row_t]
        for f in range(NF):
            product = col * w_ref[t][:, f : f + 1]
            scaled_hi = product.astype(jnp.bfloat16)
            scaled_lo = (product - scaled_hi.astype(jnp.float32)).astype(jnp.bfloat16)
            rhs_parts[f] += [scaled_hi, scaled_lo]
    lhs = jnp.concatenate(lhs_parts, axis=1)
    for f in range(NF):
        rhs = jnp.concatenate(rhs_parts[f], axis=0)
        acc_ref[f] += jnp.dot(lhs, rhs, preferred_element_type=jnp.float32)

    @pl.when(step == pl.num_programs(0) - 1)
    def _():
        for f in range(NF):
            for rho in range(subs):
                for gamma in range(subs):
                    out_ref[rho * subs + gamma, f] = acc_ref[
                        f, rho * GB : (rho + 1) * GB, gamma * GB : (gamma + 1) * GB
                    ]


def chi_block(star_map, loc, onehot, weight_c):
    rows = loc.shape[0] * loc.shape[2]
    pieces = (BW // GB) ** 2
    return pl.pallas_call(
        chi_kernel,
        out_shape=jax.ShapeDtypeStruct((pieces, NF, GB, GB), jnp.float32),
        grid_spec=pltpu.PrefetchScalarGridSpec(
            num_scalar_prefetch=1,
            grid=(KF // KB,),
            in_specs=[
                pl.BlockSpec(loc.shape, lambda st, sm: (0, 0, 0, 0)),
                pl.BlockSpec((KB, 2 * BW // GB, GB, GB), lambda st, sm: (st, 0, 0, 0)),
                pl.BlockSpec((KB, rows, NF), lambda st, sm: (st, 0, 0)),
            ],
            out_specs=pl.BlockSpec((pieces, NF, GB, GB), lambda st, sm: (0, 0, 0, 0)),
            scratch_shapes=[pltpu.VMEM((NF, BW, BW), jnp.float32)],
        ),
        compiler_params=pltpu.CompilerParams(dimension_semantics=("arbitrary",)),
    )(star_map, loc, onehot, weight_c)


def slab_perm(ka_count, band_count, ga_count):
    pieces = BW // GB
    pairs = []
    for i in range(ka_count):
        for j in range(band_count):
            for g in range(ga_count):
                row_block, col_block = BLOCKS[j][g]
                r = row_block * pieces + i // pieces
                cs = col_block * pieces + i % pieces
                src = (i * band_count + j) * ga_count + g
                dst = (cs * band_count + r // ga_count) * ga_count + r % ga_count
                pairs.append((src, dst))
    return pairs


def on_device(
    pair_density, valence_energy, conduction_energy, star_map, op_of_k, perm_lists, cond_top
):
    ka_count = lax.axis_size("ka")
    band_count = lax.axis_size("band")
    ga_count = lax.axis_size("ga")
    assert (ka_count, band_count, ga_count) == (16, 8, 2)
    ka_index = lax.axis_index("ka")
    band_index = lax.axis_index("band")
    ga_index = lax.axis_index("ga")
    cond_piece = pair_density.shape[1]
    blocks = jnp.asarray(BLOCKS, jnp.int32)

    blocked = pair_density.reshape(KI, cond_piece, NV, NB, BW)
    send = jnp.take(blocked, blocks[:, ga_index].reshape(-1), axis=3)
    send = send.reshape(KI, cond_piece, NV, band_count, 2, BW)
    send = jnp.moveaxis(send, 3, 0)
    recv = lax.all_to_all(send, "band", 0, 0, tiled=False)
    c_loc = band_count * cond_piece
    loc = recv.reshape(band_count, KI, cond_piece * NV, 2 * BW)

    c_base = ka_index * c_loc
    cond_grp = lax.dynamic_slice_in_dim(conduction_energy, c_base, c_loc, axis=1)
    cond_local = jnp.take(cond_grp, star_map, axis=0)
    val_local = jnp.take(valence_energy, star_map, axis=0)
    band_global = c_base + jnp.arange(c_loc)
    mask = (band_global[None, :] < cond_top[:, None]).astype(jnp.float32)[None, :, :, None]
    omega = freq_step * jnp.arange(NF).astype(jnp.float32)
    omega_sq = (omega * omega)[:, None, None, None]
    diff = val_local[:, None, :] - cond_local[:, :, None]
    weight = 4.0 / KF * diff[None] / (diff[None] * diff[None] + omega_sq) * mask
    weight_c = jnp.transpose(weight.reshape(NF, KF, c_loc * NV), (1, 2, 0))

    my_blocks = blocks[band_index, ga_index]
    perm_blocks = perm_lists.reshape(perm_lists.shape[0], NB, BW)
    my_perm = jnp.take(jnp.take(perm_blocks, op_of_k, axis=0), my_blocks, axis=1)
    subs = BW // GB
    local = my_perm.reshape(KF, 2 * subs, GB) - (
        my_blocks.repeat(subs) * BW + (jnp.arange(2 * subs) % subs) * GB
    )[None, :, None]
    slot = jnp.arange(GB)
    row_side = local[:, :subs, :, None] == slot[None, None, None, :]
    col_side = local[:, subs:, None, :] == slot[None, None, :, None]
    onehot = jnp.concatenate([row_side, col_side], axis=1).astype(jnp.bfloat16)
    pieces = chi_block(star_map, loc, onehot, weight_c)

    got = lax.all_to_all(pieces, "ka", 0, 0, tiled=False)
    slab = got.sum(axis=0)
    return lax.ppermute(
        slab, ("ka", "band", "ga"), slab_perm(ka_count, band_count, ga_count)
    )


def solution(mesh):
    return jax.shard_map(
        on_device,
        mesh=mesh,
        in_specs=(P(None, ("ka", "band"), None, None), P(), P(), P(), P(), P(), P()),
        out_specs=P(None, ("band", "ga"), "ka"),
        check_vma=False,
    )
```

```python
import jax
import jax.numpy as jnp
from jax import lax
from jax.experimental import pallas as pl
from jax.experimental.pallas import tpu as pltpu
from jax.sharding import PartitionSpec as P

NG = 2048
GB = 128
KI = 8
KF = 64
NF = 1
NV = 8

BW = 512
NB = NG // BW
PAIR = ((0, 1), (2, 3), (0, 1), (0, 2), (0, 3), (1, 2), (1, 3), (2, 3))
LOCAL = (((0, 0), (1, 1)), ((0, 0), (1, 1))) + (((0, 1), (1, 0)),) * 6
BLOCKS = tuple(
    tuple((PAIR[j][LOCAL[j][g][0]], PAIR[j][LOCAL[j][g][1]]) for g in range(2))
    for j in range(len(PAIR))
)
KB = 8


freq_step = 2.0


def chi_kernel(star_ref, sel_ref, loc_ref, onehot_ref, w_ref, out_ref, acc_ref):
    step = pl.program_id(0)

    @pl.when(step == 0)
    def _():
        acc_ref[...] = jnp.zeros_like(acc_ref)

    nt = (((1,), (1,)), ((), ()))
    subs = BW // GB
    lhs_parts = []
    rhs_parts = [[] for _ in range(NF)]
    for t in range(KB):
        x = loc_ref[:, star_ref[step * KB + t]]
        x = x.reshape(x.shape[0] * x.shape[1], x.shape[2])
        x_row = jnp.where(sel_ref[0] == 0, x[:, :BW], x[:, BW:])
        x_col = jnp.where(sel_ref[1] == 0, x[:, :BW], x[:, BW:])
        row_parts = []
        for q in range(subs):
            row_parts.append(
                lax.dot_general(
                    onehot_ref[t, q], x_row[:, q * GB : (q + 1) * GB], nt,
                    preferred_element_type=jnp.float32,
                )
            )
        row_t = jnp.concatenate(row_parts, axis=0).astype(jnp.bfloat16)
        col_parts = []
        for q in range(subs, 2 * subs):
            col_parts.append(
                jnp.dot(
                    x_col[:, (q - subs) * GB : (q - subs + 1) * GB], onehot_ref[t, q],
                    preferred_element_type=jnp.float32,
                )
            )
        col = jnp.concatenate(col_parts, axis=1)
        lhs_parts += [row_t, row_t]
        for f in range(NF):
            product = col * w_ref[t][:, f : f + 1]
            scaled_hi = product.astype(jnp.bfloat16)
            scaled_lo = (product - scaled_hi.astype(jnp.float32)).astype(jnp.bfloat16)
            rhs_parts[f] += [scaled_hi, scaled_lo]
    lhs = jnp.concatenate(lhs_parts, axis=1)
    for f in range(NF):
        rhs = jnp.concatenate(rhs_parts[f], axis=0)
        acc_ref[f] += jnp.dot(lhs, rhs, preferred_element_type=jnp.float32)

    @pl.when(step == pl.num_programs(0) - 1)
    def _():
        for f in range(NF):
            for rho in range(subs):
                for gamma in range(subs):
                    out_ref[rho * subs + gamma, f] = acc_ref[
                        f, rho * GB : (rho + 1) * GB, gamma * GB : (gamma + 1) * GB
                    ]


def chi_block(star_map, sel, loc, onehot, weight_c):
    rows = loc.shape[0] * loc.shape[2]
    pieces = (BW // GB) ** 2
    return pl.pallas_call(
        chi_kernel,
        out_shape=jax.ShapeDtypeStruct((pieces, NF, GB, GB), jnp.float32),
        grid_spec=pltpu.PrefetchScalarGridSpec(
            num_scalar_prefetch=2,
            grid=(KF // KB,),
            in_specs=[
                pl.BlockSpec(loc.shape, lambda st, sm, se: (0, 0, 0, 0)),
                pl.BlockSpec((KB, 2 * BW // GB, GB, GB), lambda st, sm, se: (st, 0, 0, 0)),
                pl.BlockSpec((KB, rows, NF), lambda st, sm, se: (st, 0, 0)),
            ],
            out_specs=pl.BlockSpec((pieces, NF, GB, GB), lambda st, sm, se: (0, 0, 0, 0)),
            scratch_shapes=[pltpu.VMEM((NF, BW, BW), jnp.float32)],
        ),
        compiler_params=pltpu.CompilerParams(dimension_semantics=("arbitrary",)),
    )(star_map, sel, loc, onehot, weight_c)


def slab_perm(ka_count, band_count, ga_count):
    pieces = BW // GB
    pairs = []
    for i in range(ka_count):
        for j in range(band_count):
            for g in range(ga_count):
                row_block, col_block = BLOCKS[j][g]
                r = row_block * pieces + i // pieces
                cs = col_block * pieces + i % pieces
                src = (i * band_count + j) * ga_count + g
                dst = (cs * band_count + r // ga_count) * ga_count + r % ga_count
                pairs.append((src, dst))
    return pairs


def on_device(
    pair_density, valence_energy, conduction_energy, star_map, op_of_k, perm_lists, cond_top
):
    ka_count = lax.axis_size("ka")
    band_count = lax.axis_size("band")
    ga_count = lax.axis_size("ga")
    assert (ka_count, band_count, ga_count) == (16, 8, 2)
    ka_index = lax.axis_index("ka")
    band_index = lax.axis_index("band")
    ga_index = lax.axis_index("ga")
    cond_piece = pair_density.shape[1]
    blocks = jnp.asarray(BLOCKS, jnp.int32)

    blocked = pair_density.reshape(KI, cond_piece, NV, NB, BW)
    send = jnp.stack(
        [jnp.stack([blocked[:, :, :, a], blocked[:, :, :, b]], axis=3) for a, b in PAIR]
    )
    recv = lax.all_to_all(send, "band", 0, 0, tiled=False)
    c_loc = band_count * cond_piece
    loc = recv.reshape(band_count, KI, cond_piece * NV, 2 * BW)

    c_base = ka_index * c_loc
    cond_grp = lax.dynamic_slice_in_dim(conduction_energy, c_base, c_loc, axis=1)
    cond_local = jnp.take(cond_grp, star_map, axis=0)
    val_local = jnp.take(valence_energy, star_map, axis=0)
    band_global = c_base + jnp.arange(c_loc)
    mask = (band_global[None, :] < cond_top[:, None]).astype(jnp.float32)[None, :, :, None]
    omega = freq_step * jnp.arange(NF).astype(jnp.float32)
    omega_sq = (omega * omega)[:, None, None, None]
    diff = val_local[:, None, :] - cond_local[:, :, None]
    weight = 4.0 / KF * diff[None] / (diff[None] * diff[None] + omega_sq) * mask
    weight_c = jnp.transpose(weight.reshape(NF, KF, c_loc * NV), (1, 2, 0))

    my_blocks = blocks[band_index, ga_index]
    perm_blocks = perm_lists.reshape(perm_lists.shape[0], NB, BW)
    my_perm = jnp.take(jnp.take(perm_blocks, op_of_k, axis=0), my_blocks, axis=1)
    subs = BW // GB
    local = my_perm.reshape(KF, 2 * subs, GB) - (
        my_blocks.repeat(subs) * BW + (jnp.arange(2 * subs) % subs) * GB
    )[None, :, None]
    slot = jnp.arange(GB)
    row_side = local[:, :subs, :, None] == slot[None, None, None, :]
    col_side = local[:, subs:, None, :] == slot[None, None, :, None]
    onehot = jnp.concatenate([row_side, col_side], axis=1).astype(jnp.bfloat16)
    sel = jnp.asarray(LOCAL, jnp.int32)[band_index, ga_index]
    pieces = chi_block(star_map, sel, loc, onehot, weight_c)

    got = lax.all_to_all(pieces, "ka", 0, 0, tiled=False)
    slab = got.sum(axis=0)
    return lax.ppermute(
        slab, ("ka", "band", "ga"), slab_perm(ka_count, band_count, ga_count)
    )


def solution(mesh):
    return jax.shard_map(
        on_device,
        mesh=mesh,
        in_specs=(P(None, ("ka", "band"), None, None), P(), P(), P(), P(), P(), P()),
        out_specs=P(None, ("band", "ga"), "ka"),
        check_vma=False,
    )
```

```python
import jax
import jax.numpy as jnp
from jax import lax
from jax.experimental import pallas as pl
from jax.experimental.pallas import tpu as pltpu
from jax.sharding import PartitionSpec as P


NG = 2048
GB = 128
KI = 8
KF = 64
NF = 1
NV = 8

BW = 512
NB = NG // BW
PAIR = ((0, 1), (2, 3), (0, 1), (0, 2), (0, 3), (1, 2), (1, 3), (2, 3))
LOCAL = (((0, 0), (1, 1)), ((0, 0), (1, 1))) + (((0, 1), (1, 0)),) * 6
BLOCKS = tuple(
    tuple((PAIR[j][LOCAL[j][g][0]], PAIR[j][LOCAL[j][g][1]]) for g in range(2))
    for j in range(len(PAIR))
)
KB = 8


freq_step = 2.0


def chi_kernel(star_ref, sel_ref, loc_ref, onehot_ref, w_ref, out_ref, acc_ref):
    step = pl.program_id(0)

    @pl.when(step == 0)
    def _():
        acc_ref[...] = jnp.zeros_like(acc_ref)

    nt = (((1,), (1,)), ((), ()))
    subs = BW // GB
    lhs_parts = []
    rhs_parts = [[] for _ in range(NF)]
    for t in range(KB):
        s = star_ref[step * KB + t]
        x_row = loc_ref[:, sel_ref[0], s]
        x_row = x_row.reshape(x_row.shape[0] * x_row.shape[1], BW)
        x_col = loc_ref[:, sel_ref[1], s]
        x_col = x_col.reshape(x_col.shape[0] * x_col.shape[1], BW)
        row_parts = []
        for q in range(subs):
            row_parts.append(
                lax.dot_general(
                    onehot_ref[t, q], x_row[:, q * GB : (q + 1) * GB], nt,
                    preferred_element_type=jnp.float32,
                )
            )
        row_t = jnp.concatenate(row_parts, axis=0).astype(jnp.bfloat16)
        col_parts = []
        for q in range(subs, 2 * subs):
            col_parts.append(
                jnp.dot(
                    x_col[:, (q - subs) * GB : (q - subs + 1) * GB], onehot_ref[t, q],
                    preferred_element_type=jnp.float32,
                )
            )
        col = jnp.concatenate(col_parts, axis=1)
        lhs_parts += [row_t, row_t]
        for f in range(NF):
            product = col * w_ref[t][:, f : f + 1]
            scaled_hi = product.astype(jnp.bfloat16)
            scaled_lo = (product - scaled_hi.astype(jnp.float32)).astype(jnp.bfloat16)
            rhs_parts[f] += [scaled_hi, scaled_lo]
    lhs = jnp.concatenate(lhs_parts, axis=1)
    for f in range(NF):
        rhs = jnp.concatenate(rhs_parts[f], axis=0)
        acc_ref[f] += jnp.dot(lhs, rhs, preferred_element_type=jnp.float32)

    @pl.when(step == pl.num_programs(0) - 1)
    def _():
        for f in range(NF):
            for rho in range(subs):
                for gamma in range(subs):
                    out_ref[rho * subs + gamma, f] = acc_ref[
                        f, rho * GB : (rho + 1) * GB, gamma * GB : (gamma + 1) * GB
                    ]


def chi_block(star_map, sel, loc, onehot, weight_c):
    rows = loc.shape[0] * loc.shape[3]
    pieces = (BW // GB) ** 2
    return pl.pallas_call(
        chi_kernel,
        out_shape=jax.ShapeDtypeStruct((pieces, NF, GB, GB), jnp.float32),
        grid_spec=pltpu.PrefetchScalarGridSpec(
            num_scalar_prefetch=2,
            grid=(KF // KB,),
            in_specs=[
                pl.BlockSpec(loc.shape, lambda st, sm, se: (0, 0, 0, 0, 0)),
                pl.BlockSpec((KB, 2 * BW // GB, GB, GB), lambda st, sm, se: (st, 0, 0, 0)),
                pl.BlockSpec((KB, rows, NF), lambda st, sm, se: (st, 0, 0)),
            ],
            out_specs=pl.BlockSpec((pieces, NF, GB, GB), lambda st, sm, se: (0, 0, 0, 0)),
            scratch_shapes=[pltpu.VMEM((NF, BW, BW), jnp.float32)],
        ),
        compiler_params=pltpu.CompilerParams(dimension_semantics=("arbitrary",)),
    )(star_map, sel, loc, onehot, weight_c)


def slab_perm(ka_count, band_count, ga_count):
    pieces = BW // GB
    pairs = []
    for i in range(ka_count):
        for j in range(band_count):
            for g in range(ga_count):
                row_block, col_block = BLOCKS[j][g]
                r = row_block * pieces + i // pieces
                cs = col_block * pieces + i % pieces
                src = (i * band_count + j) * ga_count + g
                dst = (cs * band_count + r // ga_count) * ga_count + r % ga_count
                pairs.append((src, dst))
    return pairs


def on_device(
    pair_density, valence_energy, conduction_energy, star_map, op_of_k, perm_lists, cond_top
):
    ka_count = lax.axis_size("ka")
    band_count = lax.axis_size("band")
    ga_count = lax.axis_size("ga")
    assert (ka_count, band_count, ga_count) == (16, 8, 2)
    ka_index = lax.axis_index("ka")
    band_index = lax.axis_index("band")
    ga_index = lax.axis_index("ga")
    cond_piece = pair_density.shape[1]
    blocks = jnp.asarray(BLOCKS, jnp.int32)

    blocked = jnp.moveaxis(pair_density.reshape(KI, cond_piece, NV, NB, BW), 3, 0)
    send = jnp.take(blocked, jnp.asarray(PAIR, jnp.int32).reshape(-1), axis=0)
    send = send.reshape(band_count, 2, KI, cond_piece, NV, BW)
    recv = lax.all_to_all(send, "band", 0, 0, tiled=False)
    c_loc = band_count * cond_piece
    loc = recv.reshape(band_count, 2, KI, cond_piece * NV, BW)

    c_base = ka_index * c_loc
    cond_grp = lax.dynamic_slice_in_dim(conduction_energy, c_base, c_loc, axis=1)
    cond_local = jnp.take(cond_grp, star_map, axis=0)
    val_local = jnp.take(valence_energy, star_map, axis=0)
    band_global = c_base + jnp.arange(c_loc)
    mask = (band_global[None, :] < cond_top[:, None]).astype(jnp.float32)[None, :, :, None]
    omega = freq_step * jnp.arange(NF).astype(jnp.float32)
    omega_sq = (omega * omega)[:, None, None, None]
    diff = val_local[:, None, :] - cond_local[:, :, None]
    weight = 4.0 / KF * diff[None] / (diff[None] * diff[None] + omega_sq) * mask
    weight_c = jnp.transpose(weight.reshape(NF, KF, c_loc * NV), (1, 2, 0))

    my_blocks = blocks[band_index, ga_index]
    perm_blocks = perm_lists.reshape(perm_lists.shape[0], NB, BW)
    my_perm = jnp.take(jnp.take(perm_blocks, op_of_k, axis=0), my_blocks, axis=1)
    subs = BW // GB
    local = my_perm.reshape(KF, 2 * subs, GB) - (
        my_blocks.repeat(subs) * BW + (jnp.arange(2 * subs) % subs) * GB
    )[None, :, None]
    slot = jnp.arange(GB)
    row_side = local[:, :subs, :, None] == slot[None, None, None, :]
    col_side = local[:, subs:, None, :] == slot[None, None, :, None]
    onehot = jnp.concatenate([row_side, col_side], axis=1).astype(jnp.bfloat16)
    sel = jnp.asarray(LOCAL, jnp.int32)[band_index, ga_index]
    pieces = chi_block(star_map, sel, loc, onehot, weight_c)

    got = lax.all_to_all(pieces, "ka", 0, 0, tiled=False)
    slab = got.sum(axis=0)
    return lax.ppermute(
        slab, ("ka", "band", "ga"), slab_perm(ka_count, band_count, ga_count)
    )


def solution(mesh):
    return jax.shard_map(
        on_device,
        mesh=mesh,
        in_specs=(P(None, ("ka", "band"), None, None), P(), P(), P(), P(), P(), P()),
        out_specs=P(None, ("band", "ga"), "ka"),
        check_vma=False,
    )
```

```python
import jax
import jax.numpy as jnp
from jax import lax
from jax.experimental import pallas as pl
from jax.experimental.pallas import tpu as pltpu
from jax.sharding import PartitionSpec as P


NG = 2048
GB = 128
KI = 8
KF = 64
NF = 1
NV = 8

BW = 512
NB = NG // BW
PAIR = ((0, 1), (2, 3), (0, 1), (0, 2), (0, 3), (1, 2), (1, 3), (2, 3))
LOCAL = (((0, 0), (1, 1)), ((0, 0), (1, 1))) + (((0, 1), (1, 0)),) * 6
BLOCKS = tuple(
    tuple((PAIR[j][LOCAL[j][g][0]], PAIR[j][LOCAL[j][g][1]]) for g in range(2))
    for j in range(len(PAIR))
)
KB = 8


freq_step = 2.0


def chi_kernel(star_ref, sel_ref, loc_ref, onehot_ref, w_ref, out_ref, acc_ref):
    step = pl.program_id(0)

    @pl.when(step == 0)
    def _():
        acc_ref[...] = jnp.zeros_like(acc_ref)

    nt = (((1,), (1,)), ((), ()))
    subs = BW // GB
    lhs_parts = []
    rhs_parts = [[] for _ in range(NF)]
    for t in range(KB):
        s = star_ref[step * KB + t]
        x_row = loc_ref[:, sel_ref[0], s]
        x_row = x_row.reshape(x_row.shape[0] * x_row.shape[1], BW)
        x_col = loc_ref[:, sel_ref[1], s]
        x_col = x_col.reshape(x_col.shape[0] * x_col.shape[1], BW)
        row_parts = []
        for q in range(subs):
            row_parts.append(
                lax.dot_general(
                    onehot_ref[t, q], x_row[:, q * GB : (q + 1) * GB], nt,
                    preferred_element_type=jnp.float32,
                )
            )
        row_t = jnp.concatenate(row_parts, axis=0).astype(jnp.bfloat16)
        col_parts = []
        for q in range(subs, 2 * subs):
            col_parts.append(
                jnp.dot(
                    x_col[:, (q - subs) * GB : (q - subs + 1) * GB], onehot_ref[t, q],
                    preferred_element_type=jnp.float32,
                )
            )
        col = jnp.concatenate(col_parts, axis=1)
        lhs_parts += [row_t, row_t]
        for f in range(NF):
            product = col * w_ref[t][:, f : f + 1]
            scaled_hi = product.astype(jnp.bfloat16)
            scaled_lo = (product - scaled_hi.astype(jnp.float32)).astype(jnp.bfloat16)
            rhs_parts[f] += [scaled_hi, scaled_lo]
    lhs = jnp.concatenate(lhs_parts, axis=1)
    for f in range(NF):
        rhs = jnp.concatenate(rhs_parts[f], axis=0)
        acc_ref[f] += jnp.dot(lhs, rhs, preferred_element_type=jnp.float32)

    @pl.when(step == pl.num_programs(0) - 1)
    def _():
        for f in range(NF):
            for rho in range(subs):
                for gamma in range(subs):
                    out_ref[rho * subs + gamma, f] = acc_ref[
                        f, rho * GB : (rho + 1) * GB, gamma * GB : (gamma + 1) * GB
                    ]


def chi_block(star_map, sel, loc, onehot, weight_c):
    rows = loc.shape[0] * loc.shape[3]
    pieces = (BW // GB) ** 2
    return pl.pallas_call(
        chi_kernel,
        out_shape=jax.ShapeDtypeStruct((pieces, NF, GB, GB), jnp.float32),
        grid_spec=pltpu.PrefetchScalarGridSpec(
            num_scalar_prefetch=2,
            grid=(KF // KB,),
            in_specs=[
                pl.BlockSpec(loc.shape, lambda st, sm, se: (0, 0, 0, 0, 0)),
                pl.BlockSpec((KB, 2 * BW // GB, GB, GB), lambda st, sm, se: (st, 0, 0, 0)),
                pl.BlockSpec((KB, rows, NF), lambda st, sm, se: (st, 0, 0)),
            ],
            out_specs=pl.BlockSpec((pieces, NF, GB, GB), lambda st, sm, se: (0, 0, 0, 0)),
            scratch_shapes=[pltpu.VMEM((NF, BW, BW), jnp.float32)],
        ),
        compiler_params=pltpu.CompilerParams(dimension_semantics=("arbitrary",)),
    )(star_map, sel, loc, onehot, weight_c)


def slab_perm(ka_count, band_count, ga_count):
    pieces = BW // GB
    pairs = []
    for i in range(ka_count):
        for j in range(band_count):
            for g in range(ga_count):
                row_block, col_block = BLOCKS[j][g]
                r = row_block * pieces + i // pieces
                cs = col_block * pieces + i % pieces
                src = (i * band_count + j) * ga_count + g
                dst = (cs * band_count + r // ga_count) * ga_count + r % ga_count
                pairs.append((src, dst))
    return pairs


def on_device(
    pair_density, valence_energy, conduction_energy, star_map, op_of_k, perm_lists, cond_top
):
    ka_count = lax.axis_size("ka")
    band_count = lax.axis_size("band")
    ga_count = lax.axis_size("ga")
    assert (ka_count, band_count, ga_count) == (16, 8, 2)
    ka_index = lax.axis_index("ka")
    band_index = lax.axis_index("band")
    ga_index = lax.axis_index("ga")
    cond_piece = pair_density.shape[1]
    blocks = jnp.asarray(BLOCKS, jnp.int32)

    blocked = jnp.moveaxis(pair_density.reshape(KI, cond_piece, NV, NB, BW), 3, 0)
    send = jnp.take(blocked, jnp.asarray(PAIR, jnp.int32).reshape(-1), axis=0)
    send = send.reshape(band_count, 2, KI, cond_piece, NV, BW)
    recv = lax.all_to_all(send, "band", 0, 0, tiled=False)
    c_loc = band_count * cond_piece
    loc = recv.reshape(band_count, 2, KI, cond_piece * NV, BW)

    c_base = ka_index * c_loc
    cond_grp = lax.dynamic_slice_in_dim(conduction_energy, c_base, c_loc, axis=1)
    cond_local = jnp.take(cond_grp, star_map, axis=0)
    val_local = jnp.take(valence_energy, star_map, axis=0)
    band_global = c_base + jnp.arange(c_loc)
    mask = (band_global[None, :] < cond_top[:, None]).astype(jnp.float32)[None, :, :, None]
    omega = freq_step * jnp.arange(NF).astype(jnp.float32)
    omega_sq = (omega * omega)[:, None, None, None]
    diff = val_local[:, None, :] - cond_local[:, :, None]
    weight = 4.0 / KF * diff[None] / (diff[None] * diff[None] + omega_sq) * mask
    weight_c = jnp.transpose(weight.reshape(NF, KF, c_loc * NV), (1, 2, 0))

    my_blocks = blocks[band_index, ga_index]
    perm_blocks = perm_lists.reshape(perm_lists.shape[0], NB, BW)
    my_perm = jnp.take(jnp.take(perm_blocks, op_of_k, axis=0), my_blocks, axis=1)
    subs = BW // GB
    local = my_perm.reshape(KF, 2 * subs, GB) - (
        my_blocks.repeat(subs) * BW + (jnp.arange(2 * subs) % subs) * GB
    )[None, :, None]
    slot = jnp.arange(GB)
    row_side = local[:, :, :, None] == slot[None, None, None, :]
    col_side = local[:, :, None, :] == slot[None, None, :, None]
    is_row = (jnp.arange(2 * subs) < subs)[None, :, None, None]
    onehot = jnp.where(
        jnp.where(is_row, row_side, col_side), jnp.bfloat16(1), jnp.bfloat16(0)
    )
    sel = jnp.asarray(LOCAL, jnp.int32)[band_index, ga_index]
    pieces = chi_block(star_map, sel, loc, onehot, weight_c)

    got = lax.all_to_all(pieces, "ka", 0, 0, tiled=False)
    slab = got.sum(axis=0)
    return lax.ppermute(
        slab, ("ka", "band", "ga"), slab_perm(ka_count, band_count, ga_count)
    )


def solution(mesh):
    return jax.shard_map(
        on_device,
        mesh=mesh,
        in_specs=(P(None, ("ka", "band"), None, None), P(), P(), P(), P(), P(), P()),
        out_specs=P(None, ("band", "ga"), "ka"),
        check_vma=False,
    )
```

```python
import jax
import jax.numpy as jnp
from jax import lax
from jax.experimental import pallas as pl
from jax.experimental.pallas import tpu as pltpu
from jax.sharding import PartitionSpec as P


NG = 2048
GB = 128
KI = 8
KF = 64
NF = 1
NV = 8

BW = 512
NB = NG // BW
PAIR = ((0, 1), (2, 3), (0, 1), (0, 2), (0, 3), (1, 2), (1, 3), (2, 3))
LOCAL = (((0, 0), (1, 1)), ((0, 0), (1, 1))) + (((0, 1), (1, 0)),) * 6
BLOCKS = tuple(
    tuple((PAIR[j][LOCAL[j][g][0]], PAIR[j][LOCAL[j][g][1]]) for g in range(2))
    for j in range(len(PAIR))
)
KB = 16


freq_step = 2.0


def chi_kernel(star_ref, sel_ref, loc_ref, onehot_ref, w_ref, out_ref, acc_ref, row_ref, hi_ref, lo_ref):
    step = pl.program_id(0)

    @pl.when(step == 0)
    def _():
        acc_ref[...] = jnp.zeros_like(acc_ref)

    nt = (((1,), (1,)), ((), ()))
    subs = BW // GB
    for f in range(NF):
        for t in range(KB):
            s = star_ref[step * KB + t]
            x_row = loc_ref[:, sel_ref[0], s]
            x_row = x_row.reshape(x_row.shape[0] * x_row.shape[1], BW)
            x_col = loc_ref[:, sel_ref[1], s]
            x_col = x_col.reshape(x_col.shape[0] * x_col.shape[1], BW)
            rows = x_row.shape[0]
            if f == 0:
                for q in range(subs):
                    row_ref[q * GB : (q + 1) * GB, t * rows : (t + 1) * rows] = lax.dot_general(
                        onehot_ref[t, q], x_row[:, q * GB : (q + 1) * GB], nt,
                        preferred_element_type=jnp.float32,
                    ).astype(jnp.bfloat16)
            col_parts = []
            for q in range(subs, 2 * subs):
                col_parts.append(
                    jnp.dot(
                        x_col[:, (q - subs) * GB : (q - subs + 1) * GB], onehot_ref[t, q],
                        preferred_element_type=jnp.float32,
                    )
                )
            col = jnp.concatenate(col_parts, axis=1)
            product = col * w_ref[t][:, f : f + 1]
            scaled_hi = product.astype(jnp.bfloat16)
            hi_ref[t * rows : (t + 1) * rows, :] = scaled_hi
            lo_ref[t * rows : (t + 1) * rows, :] = (
                product - scaled_hi.astype(jnp.float32)
            ).astype(jnp.bfloat16)
        lhs = row_ref[...]
        acc_ref[f] += jnp.dot(lhs, hi_ref[...], preferred_element_type=jnp.float32) + jnp.dot(
            lhs, lo_ref[...], preferred_element_type=jnp.float32
        )

    @pl.when(step == pl.num_programs(0) - 1)
    def _():
        for f in range(NF):
            for rho in range(subs):
                for gamma in range(subs):
                    out_ref[rho * subs + gamma, f] = acc_ref[
                        f, rho * GB : (rho + 1) * GB, gamma * GB : (gamma + 1) * GB
                    ]


def chi_block(star_map, sel, loc, onehot, weight_c):
    rows = loc.shape[0] * loc.shape[3]
    pieces = (BW // GB) ** 2
    return pl.pallas_call(
        chi_kernel,
        out_shape=jax.ShapeDtypeStruct((pieces, NF, GB, GB), jnp.float32),
        grid_spec=pltpu.PrefetchScalarGridSpec(
            num_scalar_prefetch=2,
            grid=(KF // KB,),
            in_specs=[
                pl.BlockSpec(loc.shape, lambda st, sm, se: (0, 0, 0, 0, 0)),
                pl.BlockSpec((KB, 2 * BW // GB, GB, GB), lambda st, sm, se: (st, 0, 0, 0)),
                pl.BlockSpec((KB, rows, GB), lambda st, sm, se: (st, 0, 0)),
            ],
            out_specs=pl.BlockSpec((pieces, NF, GB, GB), lambda st, sm, se: (0, 0, 0, 0)),
            scratch_shapes=[
                pltpu.VMEM((NF, BW, BW), jnp.float32),
                pltpu.VMEM((BW, KB * rows), jnp.bfloat16),
                pltpu.VMEM((KB * rows, BW), jnp.bfloat16),
                pltpu.VMEM((KB * rows, BW), jnp.bfloat16),
            ],
        ),
        compiler_params=pltpu.CompilerParams(dimension_semantics=("arbitrary",)),
    )(star_map, sel, loc, onehot, weight_c)


def slab_perm(ka_count, band_count, ga_count):
    pieces = BW // GB
    pairs = []
    for i in range(ka_count):
        for j in range(band_count):
            for g in range(ga_count):
                row_block, col_block = BLOCKS[j][g]
                r = row_block * pieces + i // pieces
                cs = col_block * pieces + i % pieces
                src = (i * band_count + j) * ga_count + g
                dst = (cs * band_count + r // ga_count) * ga_count + r % ga_count
                pairs.append((src, dst))
    return pairs


def on_device(
    pair_density, valence_energy, conduction_energy, star_map, op_of_k, perm_lists, cond_top
):
    ka_count = lax.axis_size("ka")
    band_count = lax.axis_size("band")
    ga_count = lax.axis_size("ga")
    assert (ka_count, band_count, ga_count) == (16, 8, 2)
    ka_index = lax.axis_index("ka")
    band_index = lax.axis_index("band")
    ga_index = lax.axis_index("ga")
    cond_piece = pair_density.shape[1]
    blocks = jnp.asarray(BLOCKS, jnp.int32)

    blocked = jnp.moveaxis(pair_density.reshape(KI, cond_piece, NV, NB, BW), 3, 0)
    send = jnp.take(blocked, jnp.asarray(PAIR, jnp.int32).reshape(-1), axis=0)
    send = send.reshape(band_count, 2, KI, cond_piece, NV, BW)
    recv = lax.all_to_all(send, "band", 0, 0, tiled=False)
    c_loc = band_count * cond_piece
    loc = recv.reshape(band_count, 2, KI, cond_piece * NV, BW)

    c_base = ka_index * c_loc
    cond_grp = lax.dynamic_slice_in_dim(conduction_energy, c_base, c_loc, axis=1)
    cond_local = jnp.take(cond_grp, star_map, axis=0)
    val_local = jnp.take(valence_energy, star_map, axis=0)
    band_global = c_base + jnp.arange(c_loc)
    mask = (band_global[None, :] < cond_top[:, None]).astype(jnp.float32)[None, :, :, None]
    omega = freq_step * jnp.arange(NF).astype(jnp.float32)
    omega_sq = (omega * omega)[:, None, None, None]
    diff = val_local[:, None, :] - cond_local[:, :, None]
    weight = 4.0 / KF * diff[None] / (diff[None] * diff[None] + omega_sq) * mask
    weight_c = jnp.broadcast_to(
        jnp.transpose(weight.reshape(NF, KF, c_loc * NV), (1, 2, 0)), (KF, c_loc * NV, GB)
    )

    my_blocks = blocks[band_index, ga_index]
    perm_blocks = perm_lists.reshape(perm_lists.shape[0], NB, BW)
    my_perm = jnp.take(jnp.take(perm_blocks, op_of_k, axis=0), my_blocks, axis=1)
    subs = BW // GB
    local = my_perm.reshape(KF, 2 * subs, GB) - (
        my_blocks.repeat(subs) * BW + (jnp.arange(2 * subs) % subs) * GB
    )[None, :, None]
    slot = jnp.arange(GB)
    row_side = local[:, :, :, None] == slot[None, None, None, :]
    col_side = local[:, :, None, :] == slot[None, None, :, None]
    is_row = (jnp.arange(2 * subs) < subs)[None, :, None, None]
    onehot = jnp.where(
        jnp.where(is_row, row_side, col_side), jnp.bfloat16(1), jnp.bfloat16(0)
    )
    sel = jnp.asarray(LOCAL, jnp.int32)[band_index, ga_index]
    pieces = chi_block(star_map, sel, loc, onehot, weight_c)

    got = lax.all_to_all(pieces, "ka", 0, 0, tiled=False)
    slab = got.sum(axis=0)
    return lax.ppermute(
        slab, ("ka", "band", "ga"), slab_perm(ka_count, band_count, ga_count)
    )


def solution(mesh):
    return jax.shard_map(
        on_device,
        mesh=mesh,
        in_specs=(P(None, ("ka", "band"), None, None), P(), P(), P(), P(), P(), P()),
        out_specs=P(None, ("band", "ga"), "ka"),
        check_vma=False,
    )
```

```python
import jax
import jax.numpy as jnp
from jax import lax
from jax.experimental import pallas as pl
from jax.experimental.pallas import tpu as pltpu
from jax.sharding import PartitionSpec as P


NG = 2048
GB = 128
KI = 8
KF = 64
NF = 1
NV = 8

BW = 512
NB = NG // BW
PAIR = ((0, 1), (2, 3), (0, 1), (0, 2), (0, 3), (1, 2), (1, 3), (2, 3))
LOCAL = (((0, 0), (1, 1)), ((0, 0), (1, 1))) + (((0, 1), (1, 0)),) * 6
BLOCKS = tuple(
    tuple((PAIR[j][LOCAL[j][g][0]], PAIR[j][LOCAL[j][g][1]]) for g in range(2))
    for j in range(len(PAIR))
)
KB = 8


freq_step = 2.0


def chi_kernel(star_ref, sel_ref, loc_ref, onehot_ref, w_ref, out_ref, acc_ref):
    step = pl.program_id(0)

    @pl.when(step == 0)
    def _():
        acc_ref[...] = jnp.zeros_like(acc_ref)

    nt = (((1,), (1,)), ((), ()))
    subs = BW // GB
    lhs_parts = []
    rhs_parts = [[] for _ in range(NF)]
    for t in range(KB):
        s = star_ref[step * KB + t]
        x_row = loc_ref[:, sel_ref[0], s]
        x_row = x_row.reshape(x_row.shape[0] * x_row.shape[1], BW)
        x_col = loc_ref[:, sel_ref[1], s]
        x_col = x_col.reshape(x_col.shape[0] * x_col.shape[1], BW)
        row_parts = []
        for q in range(subs):
            row_parts.append(
                lax.dot_general(
                    onehot_ref[t, q], x_row[:, q * GB : (q + 1) * GB], nt,
                    preferred_element_type=jnp.float32,
                )
            )
        row_t = jnp.concatenate(row_parts, axis=0).astype(jnp.bfloat16)
        col_parts = []
        for q in range(subs, 2 * subs):
            col_parts.append(
                jnp.dot(
                    x_col[:, (q - subs) * GB : (q - subs + 1) * GB], onehot_ref[t, q],
                    preferred_element_type=jnp.float32,
                )
            )
        col = jnp.concatenate(col_parts, axis=1)
        lhs_parts += [row_t, row_t]
        for f in range(NF):
            product = col * w_ref[t][:, f : f + 1]
            scaled_hi = product.astype(jnp.bfloat16)
            scaled_lo = (product - scaled_hi.astype(jnp.float32)).astype(jnp.bfloat16)
            rhs_parts[f] += [scaled_hi, scaled_lo]
    lhs = jnp.concatenate(lhs_parts, axis=1)
    for f in range(NF):
        rhs = jnp.concatenate(rhs_parts[f], axis=0)
        acc_ref[f] += jnp.dot(lhs, rhs, preferred_element_type=jnp.float32)

    @pl.when(step == pl.num_programs(0) - 1)
    def _():
        for f in range(NF):
            for rho in range(subs):
                for gamma in range(subs):
                    out_ref[rho * subs + gamma, f] = acc_ref[
                        f, rho * GB : (rho + 1) * GB, gamma * GB : (gamma + 1) * GB
                    ]


def chi_block(star_map, sel, loc, onehot, weight_c):
    rows = loc.shape[0] * loc.shape[3]
    pieces = (BW // GB) ** 2
    return pl.pallas_call(
        chi_kernel,
        out_shape=jax.ShapeDtypeStruct((pieces, NF, GB, GB), jnp.float32),
        grid_spec=pltpu.PrefetchScalarGridSpec(
            num_scalar_prefetch=2,
            grid=(KF // KB,),
            in_specs=[
                pl.BlockSpec(memory_space=pltpu.VMEM),
                pl.BlockSpec((KB, 2 * BW // GB, GB, GB), lambda st, sm, se: (st, 0, 0, 0)),
                pl.BlockSpec((KB, rows, GB), lambda st, sm, se: (st, 0, 0)),
            ],
            out_specs=pl.BlockSpec((pieces, NF, GB, GB), lambda st, sm, se: (0, 0, 0, 0)),
            scratch_shapes=[pltpu.VMEM((NF, BW, BW), jnp.float32)],
        ),
        compiler_params=pltpu.CompilerParams(dimension_semantics=("arbitrary",)),
    )(star_map, sel, loc, onehot, weight_c)


def slab_perm(ka_count, band_count, ga_count):
    pieces = BW // GB
    pairs = []
    for i in range(ka_count):
        for j in range(band_count):
            for g in range(ga_count):
                row_block, col_block = BLOCKS[j][g]
                r = row_block * pieces + i // pieces
                cs = col_block * pieces + i % pieces
                src = (i * band_count + j) * ga_count + g
                dst = (cs * band_count + r // ga_count) * ga_count + r % ga_count
                pairs.append((src, dst))
    return pairs


def on_device(
    pair_density, valence_energy, conduction_energy, star_map, op_of_k, perm_lists, cond_top
):
    ka_count = lax.axis_size("ka")
    band_count = lax.axis_size("band")
    ga_count = lax.axis_size("ga")
    assert (ka_count, band_count, ga_count) == (16, 8, 2)
    ka_index = lax.axis_index("ka")
    band_index = lax.axis_index("band")
    ga_index = lax.axis_index("ga")
    cond_piece = pair_density.shape[1]
    blocks = jnp.asarray(BLOCKS, jnp.int32)

    blocked = jnp.moveaxis(pair_density.reshape(KI, cond_piece, NV, NB, BW), 3, 0)
    send = jnp.take(blocked, jnp.asarray(PAIR, jnp.int32).reshape(-1), axis=0)
    send = send.reshape(band_count, 2, KI, cond_piece, NV, BW)
    recv = lax.all_to_all(send, "band", 0, 0, tiled=False)
    c_loc = band_count * cond_piece
    loc = recv.reshape(band_count, 2, KI, cond_piece * NV, BW)

    c_base = ka_index * c_loc
    cond_grp = lax.dynamic_slice_in_dim(conduction_energy, c_base, c_loc, axis=1)
    cond_local = jnp.take(cond_grp, star_map, axis=0)
    val_local = jnp.take(valence_energy, star_map, axis=0)
    band_global = c_base + jnp.arange(c_loc)
    mask = (band_global[None, :] < cond_top[:, None]).astype(jnp.float32)[None, :, :, None]
    omega = freq_step * jnp.arange(NF).astype(jnp.float32)
    omega_sq = (omega * omega)[:, None, None, None]
    diff = val_local[:, None, :] - cond_local[:, :, None]
    weight = 4.0 / KF * diff[None] / (diff[None] * diff[None] + omega_sq) * mask
    weight_c = jnp.broadcast_to(
        jnp.transpose(weight.reshape(NF, KF, c_loc * NV), (1, 2, 0)), (KF, c_loc * NV, GB)
    )

    my_blocks = blocks[band_index, ga_index]
    perm_blocks = perm_lists.reshape(perm_lists.shape[0], NB, BW)
    my_perm = jnp.take(jnp.take(perm_blocks, op_of_k, axis=0), my_blocks, axis=1)
    subs = BW // GB
    local = my_perm.reshape(KF, 2 * subs, GB) - (
        my_blocks.repeat(subs) * BW + (jnp.arange(2 * subs) % subs) * GB
    )[None, :, None]
    slot = jnp.arange(GB)
    row_side = local[:, :, :, None] == slot[None, None, None, :]
    col_side = local[:, :, None, :] == slot[None, None, :, None]
    is_row = (jnp.arange(2 * subs) < subs)[None, :, None, None]
    onehot = jnp.where(
        jnp.where(is_row, row_side, col_side), jnp.bfloat16(1), jnp.bfloat16(0)
    )
    sel = jnp.asarray(LOCAL, jnp.int32)[band_index, ga_index]
    pieces = chi_block(star_map, sel, loc, onehot, weight_c)

    got = lax.all_to_all(pieces, "ka", 0, 0, tiled=False)
    slab = got.sum(axis=0)
    return lax.ppermute(
        slab, ("ka", "band", "ga"), slab_perm(ka_count, band_count, ga_count)
    )


def solution(mesh):
    return jax.shard_map(
        on_device,
        mesh=mesh,
        in_specs=(P(None, ("ka", "band"), None, None), P(), P(), P(), P(), P(), P()),
        out_specs=P(None, ("band", "ga"), "ka"),
        check_vma=False,
    )
```
